32 devices in a mesh: dp: 8 (over z, x), group: 4 (over y, core).
Axes of the slice: x: 2, y: 2, z: 4, core: 2. Of those that a mesh axis runs over, the one named last changes fastest.
Arguments:
- partials: float32 [4, 54, 1024, 1024], P('group', None, 'dp'), may hold values from -0.3 to 0.3
- second_moment: float32 [54, 1024, 1024], P(None, 'dp', 'group'), may hold values from 0.0001 to 0.01
- left_stats: float32 [54, 1024, 1024], P(None, 'dp', 'group'), may hold values from -3 to 3
- right_stats: float32 [54, 1024, 1024], P(None, 'dp', 'group'), may hold values from -3 to 3
- left_roots: bfloat16 [54, 1024, 1024], P(None, 'dp', 'group'), may hold values from -0.2 to 2.1
- right_roots: bfloat16 [54, 1024, 1024], P(None, 'dp', 'group'), may hold values from -0.2 to 2.1
- norm_partials: float32 [8, 4, 2, 2048], P('dp', 'group'), may hold values from -0.012 to 0.012
- norm_moment: float32 [2, 2048], replicated, may hold values from 0.0001 to 0.01
Outputs:
- block_step: bfloat16 [54, 1024, 1024], P(None, 'dp', 'group')
- new_moment: float32 [54, 1024, 1024], P(None, 'dp', 'group')
- new_left: float32 [54, 1024, 1024], P(None, 'dp', 'group')
- new_right: float32 [54, 1024, 1024], P(None, 'dp', 'group')
- norm_step: float32 [2, 2048], replicated
- new_norm_moment: float32 [2, 2048], replicated
The draws below stay inside these ranges and needn't reach their ends.
All inputs are finite; a program needn't handle non-finite values.
Results may differ from the reference program's by a relative error of at most 0.0042.
The reference program's roundings to bfloat16 on the way (of `grad_low` and `half`) count: a program that leaves them out, or rounds other values in their place, can miss the bound.
Values may be sent and summed in bfloat16 or wider, within the bound.
No kernel may reach another device: no remote copies, remote signals or barrier semaphores. Data moves between devices by JAX's collectives and lax.ppermute only.
A program may use at most 384 MiB of HBM per device.

```python
import math
import jax
import jax.numpy as jnp
from jax import lax

B = 1024
D = 2048
NB = 54
N_DP = 8
N_GROUP = 4


def draw_root_table(key):
    noise_key, diag_key = jax.random.split(key)
    shape = (NB, B, B)
    rows = jax.lax.broadcasted_iota(jnp.int32, shape, 1)
    cols = jax.lax.broadcasted_iota(jnp.int32, shape, 2)
    off = jnp.clip(jax.random.normal(noise_key, shape, jnp.float32) * (0.7 / math.sqrt(B)), -0.12, 0.12)
    diag = jnp.exp(jax.random.uniform(diag_key, shape, jnp.float32, -0.69, 0.69))
    return jnp.where(rows == cols, diag, off).astype(jnp.bfloat16)


def draw_left_roots(key, part):
    return draw_root_table(jax.random.fold_in(key, 11))


def draw_right_roots(key, part):
    return draw_root_table(jax.random.fold_in(key, 23))


def levels(rng, dims, cuts, smallest, high):
    def one(dim, parts):
        heights = jax.random.uniform(jax.random.fold_in(jax.random.fold_in(rng, 6), dim), (parts,), jnp.float32, smallest / len(cuts), high / len(cuts))
        return jnp.repeat(jnp.exp(heights), dims[dim] // parts).reshape((-1,) + (1,) * (len(dims) - dim - 1))

    factor_of = one(*cuts[0])
    for cut in cuts[1:]:
        factor_of = factor_of * one(*cut)
    return factor_of


def centred(key, extent, spread, reach, shards=(), kind=jnp.bfloat16):
    entries = spread * jax.random.normal(key, extent, jnp.float32)
    if shards:
        entries = entries * levels(key, extent, shards, -0.22, 0.18)
    return jnp.clip(entries, -reach, reach).astype(kind)


def setup_inputs(seed: int = 0) -> dict:
    key_list = jax.random.split(jax.random.key(seed), 9)
    partials = centred(key_list[0], (N_GROUP, NB, B, B), 0.05, 0.3, ((0, 4), (2, 8)), jnp.float32)
    second_moment = jnp.clip(jnp.exp(math.log(0.01) - 4.6051702 * jax.random.uniform(key_list[1], (NB, B, B), jnp.float32) ** levels(key_list[1], (NB, B, B), ((1, 8), (2, 4)), -0.2, 0.2)), 0.0001, 0.01)
    left_stats = centred(key_list[2], (NB, B, B), 0.5, 3.0, ((1, 8), (2, 4)), jnp.float32)
    right_stats = centred(key_list[3], (NB, B, B), 0.5, 3.0, ((1, 8), (2, 4)), jnp.float32)
    left_roots = draw_left_roots(jax.random.fold_in(key_list[8], 71), 0)
    right_roots = draw_right_roots(jax.random.fold_in(key_list[8], 71), 0)
    norm_partials = centred(key_list[6], (N_DP, N_GROUP, 2, D), 0.002, 0.012, ((0, 8), (1, 4)), jnp.float32)
    norm_moment = jnp.clip(jnp.exp(jax.random.uniform(key_list[7], (2, D), jnp.float32, math.log(0.0001), math.log(0.01))), 0.0001, 0.01)
    return {"partials": partials, "second_moment": second_moment, "left_stats": left_stats, "right_stats": right_stats, "left_roots": left_roots, "right_roots": right_roots, "norm_partials": norm_partials, "norm_moment": norm_moment}


def reference(partials, second_moment, left_stats, right_stats, left_roots, right_roots, norm_partials, norm_moment):
    grad = lax.optimization_barrier(jnp.sum(partials, axis=0))
    new_moment = 0.99 * second_moment + 0.01 * grad * grad
    adam = grad / (jnp.sqrt(new_moment) + 1e-08)
    adam_sq = lax.optimization_barrier(jnp.sum(adam * adam, axis=(1, 2)))
    grad_low = grad.astype(jnp.bfloat16)

    def one_block(index):
        block = grad_low[index]
        left_root = left_roots[index]
        right_root = right_roots[index]
        gram_left = jnp.dot(block, block.T, preferred_element_type=jnp.float32)
        gram_right = jnp.dot(block.T, block, preferred_element_type=jnp.float32)
        half = jnp.dot(block, right_root, preferred_element_type=jnp.float32).astype(jnp.bfloat16)
        direction = jnp.dot(left_root, half, preferred_element_type=jnp.float32)
        ratio = jnp.sqrt(adam_sq[index] / (jnp.sum(direction * direction) + 1e-06))
        return (gram_left, gram_right, (ratio * direction).astype(jnp.bfloat16))
    gram_left, gram_right, block_step = lax.map(one_block, jnp.arange(NB, dtype=jnp.int32))
    new_left = 0.95 * left_stats + 0.05 * gram_left
    new_right = 0.95 * right_stats + 0.05 * gram_right
    norm_grad = lax.optimization_barrier(jnp.sum(norm_partials, axis=(0, 1)))
    new_norm_moment = 0.99 * norm_moment + 0.01 * norm_grad * norm_grad
    norm_step = norm_grad / (jnp.sqrt(new_norm_moment) + 1e-08)
    return (block_step, new_moment, new_left, new_right, norm_step, new_norm_moment)
```

```python
import jax
import jax.numpy as jnp
from jax import lax
from jax.sharding import PartitionSpec as P

EPS_ADAM = 1e-08
EPS_GRAFT = 1e-06


def on_device(
    partials,
    second_moment,
    left_stats,
    right_stats,
    left_roots,
    right_roots,
    norm_partials,
    norm_moment,
):
    n_dp = lax.axis_size("dp")
    me_dp = lax.axis_index("dp")
    me_group = lax.axis_index("group")
    count = second_moment.shape[0]
    rows = partials.shape[2]
    quarter = second_moment.shape[2]
    width = rows * n_dp
    cap = -(-count // n_dp)
    slots = cap * n_dp
    lower = me_group * quarter

    def to_owners(blocks):
        padded = jnp.pad(blocks, ((0, slots - count), (0, 0), (0, 0)))
        sent = lax.all_to_all(padded.reshape(n_dp, cap, rows, quarter), "dp", 0, 0, tiled=True)
        return sent.transpose(1, 0, 2, 3).reshape(cap, width, quarter)

    def to_keepers(owned):
        back = lax.all_to_all(owned, "dp", 0, 0, tiled=True)
        return back.reshape(slots, rows, quarter)[:count]

    left_root = to_owners(left_roots)
    right_root = to_owners(right_roots)

    local_norm = norm_partials[0, 0]
    norm_grad = lax.psum(local_norm, ("dp", "group"))
    grad = lax.psum_scatter(partials[0], "group", scatter_dimension=2, tiled=True)
    new_moment = 0.99 * second_moment + 0.01 * grad * grad
    adam = grad / (jnp.sqrt(new_moment) + EPS_ADAM)
    adam_part = jnp.sum(adam * adam, axis=(1, 2))
    adam_sq = lax.psum(adam_part, ("dp", "group"))
    grad_low = grad.astype(jnp.bfloat16)

    mine = to_owners(grad_low)
    piece = lax.all_gather(mine, "group", axis=2, tiled=True)
    own_rows = lax.dynamic_slice_in_dim(piece, lower, quarter, 1)
    piece4 = piece.reshape(cap, n_dp, rows, width)
    gram_left = jnp.einsum("cdim,cjm->dcij", piece4, own_rows, preferred_element_type=jnp.float32)
    gram_right = jnp.einsum("cim,cij->cmj", piece, mine, preferred_element_type=jnp.float32)
    gram_right = gram_right.reshape(cap, n_dp, rows, quarter).transpose(1, 0, 2, 3)
    left_term = to_keepers(gram_left.astype(jnp.bfloat16)).astype(jnp.float32)
    right_term = to_keepers(gram_right.astype(jnp.bfloat16)).astype(jnp.float32)

    half = jnp.einsum("cim,cmj->cij", piece, right_root, preferred_element_type=jnp.float32)
    half = half.astype(jnp.bfloat16)
    full_left = lax.all_gather(left_root, "group", axis=2, tiled=True)
    full_left4 = full_left.reshape(cap, n_dp, rows, width)
    direction = jnp.einsum("cdim,cmj->dcij", full_left4, half, preferred_element_type=jnp.float32)
    direction_sq = lax.psum(jnp.sum(direction * direction, axis=(0, 2, 3)), "group")
    adam_pad = jnp.pad(adam_sq, (0, slots - count))
    adam_owned = lax.dynamic_slice_in_dim(adam_pad, me_dp * cap, cap)
    ratio = jnp.sqrt(adam_owned / (direction_sq + EPS_GRAFT))
    scaled = (ratio[None, :, None, None] * direction).astype(jnp.bfloat16)
    block_step = to_keepers(scaled)

    new_left = 0.95 * left_stats + 0.05 * left_term
    new_right = 0.95 * right_stats + 0.05 * right_term
    new_norm_moment = 0.99 * norm_moment + 0.01 * norm_grad * norm_grad
    norm_step = norm_grad / (jnp.sqrt(new_norm_moment) + EPS_ADAM)
    return (block_step, new_moment, new_left, new_right, norm_step, new_norm_moment)


def solution(mesh):
    return jax.shard_map(
        on_device,
        mesh=mesh,
        in_specs=(
            P("group", None, "dp", None),
            P(None, "dp", "group"),
            P(None, "dp", "group"),
            P(None, "dp", "group"),
            P(None, "dp", "group"),
            P(None, "dp", "group"),
            P("dp", "group", None, None),
            P(),
        ),
        out_specs=(
            P(None, "dp", "group"),
            P(None, "dp", "group"),
            P(None, "dp", "group"),
            P(None, "dp", "group"),
            P(),
            P(),
        ),
        check_vma=False,
    )
```

```python
import jax
import jax.numpy as jnp
from jax import lax
from jax.sharding import PartitionSpec as P

EPS_ADAM = 1e-08
EPS_GRAFT = 1e-06


def on_device(
    partials,
    second_moment,
    left_stats,
    right_stats,
    left_roots,
    right_roots,
    norm_partials,
    norm_moment,
):
    n_dp = lax.axis_size("dp")
    me_dp = lax.axis_index("dp")
    me_group = lax.axis_index("group")
    count = second_moment.shape[0]
    rows = partials.shape[2]
    quarter = second_moment.shape[2]
    width = rows * n_dp
    cap = -(-count // n_dp)
    slots = cap * n_dp
    lower = me_group * quarter

    def to_owners(blocks):
        padded = jnp.pad(blocks, ((0, slots - count), (0, 0), (0, 0)))
        sent = lax.all_to_all(padded.reshape(n_dp, cap, rows, quarter), "dp", 0, 0, tiled=True)
        return sent.transpose(1, 0, 2, 3).reshape(cap, width, quarter)

    def to_keepers(owned):
        back = lax.all_to_all(owned, "dp", 0, 0, tiled=True)
        return back.reshape(slots, rows, quarter)[:count]

    left_root = to_owners(left_roots)
    right_root = to_owners(right_roots)

    local_norm = norm_partials[0, 0]
    norm_grad = jnp.sum(lax.all_gather(local_norm, ("dp", "group")), axis=0)
    grad = lax.psum_scatter(partials[0], "group", scatter_dimension=2, tiled=True)
    grad, left_root, right_root = lax.optimization_barrier((grad, left_root, right_root))
    new_moment = 0.99 * second_moment + 0.01 * grad * grad
    adam = grad / (jnp.sqrt(new_moment) + EPS_ADAM)
    adam_part = jnp.sum(adam * adam, axis=(1, 2))
    adam_sq = jnp.sum(lax.all_gather(adam_part, ("dp", "group")), axis=0)
    grad_low = grad.astype(jnp.bfloat16)

    mine = to_owners(grad_low)
    piece = lax.all_gather(mine, "group", axis=2, tiled=True)
    own_rows = lax.dynamic_slice_in_dim(piece, lower, quarter, 1)
    piece4 = piece.reshape(cap, n_dp, rows, width)
    gram_left = jnp.einsum("cdim,cjm->dcij", piece4, own_rows, preferred_element_type=jnp.float32)
    gram_right = jnp.einsum("cim,cij->cmj", piece, mine, preferred_element_type=jnp.float32)
    gram_right = gram_right.reshape(cap, n_dp, rows, quarter).transpose(1, 0, 2, 3)
    left_term = to_keepers(gram_left.astype(jnp.bfloat16)).astype(jnp.float32)
    right_term = to_keepers(gram_right.astype(jnp.bfloat16)).astype(jnp.float32)

    half = jnp.einsum("cim,cmj->cij", piece, right_root, preferred_element_type=jnp.float32)
    half = half.astype(jnp.bfloat16)
    full_left = lax.all_gather(left_root, "group", axis=2, tiled=True)
    full_left4 = full_left.reshape(cap, n_dp, rows, width)
    direction = jnp.einsum("cdim,cmj->dcij", full_left4, half, preferred_element_type=jnp.float32)
    direction_sq = lax.psum(jnp.sum(direction * direction, axis=(0, 2, 3)), "group")
    adam_pad = jnp.pad(adam_sq, (0, slots - count))
    adam_owned = lax.dynamic_slice_in_dim(adam_pad, me_dp * cap, cap)
    ratio = jnp.sqrt(adam_owned / (direction_sq + EPS_GRAFT))
    scaled = (ratio[None, :, None, None] * direction).astype(jnp.bfloat16)
    block_step = to_keepers(scaled)

    new_left = 0.95 * left_stats + 0.05 * left_term
    new_right = 0.95 * right_stats + 0.05 * right_term
    new_norm_moment = 0.99 * norm_moment + 0.01 * norm_grad * norm_grad
    norm_step = norm_grad / (jnp.sqrt(new_norm_moment) + EPS_ADAM)
    return (block_step, new_moment, new_left, new_right, norm_step, new_norm_moment)


def solution(mesh):
    return jax.shard_map(
        on_device,
        mesh=mesh,
        in_specs=(
            P("group", None, "dp", None),
            P(None, "dp", "group"),
            P(None, "dp", "group"),
            P(None, "dp", "group"),
            P(None, "dp", "group"),
            P(None, "dp", "group"),
            P("dp", "group", None, None),
            P(),
        ),
        out_specs=(
            P(None, "dp", "group"),
            P(None, "dp", "group"),
            P(None, "dp", "group"),
            P(None, "dp", "group"),
            P(),
            P(),
        ),
        check_vma=False,
    )
```

```python
import jax
import jax.numpy as jnp
from jax import lax
from jax.sharding import PartitionSpec as P

EPS_ADAM = 1e-08
EPS_GRAFT = 1e-06


def on_device(
    partials,
    second_moment,
    left_stats,
    right_stats,
    left_roots,
    right_roots,
    norm_partials,
    norm_moment,
):
    n_dp = lax.axis_size("dp")
    me_dp = lax.axis_index("dp")
    me_group = lax.axis_index("group")
    count = second_moment.shape[0]
    rows = partials.shape[2]
    quarter = second_moment.shape[2]
    width = rows * n_dp
    cap = -(-count // n_dp)
    slots = cap * n_dp
    lower = me_group * quarter

    def to_owners(blocks):
        padded = jnp.pad(blocks, ((0, slots - count), (0, 0), (0, 0)))
        sent = lax.all_to_all(padded.reshape(n_dp, cap, rows, quarter), "dp", 0, 0, tiled=True)
        return sent.transpose(1, 0, 2, 3).reshape(cap, width, quarter)

    def to_keepers(owned):
        back = lax.all_to_all(owned, "dp", 0, 0, tiled=True)
        return back.reshape(slots, rows, quarter)[:count]

    left_root = to_owners(left_roots)
    right_root = to_owners(right_roots)

    local_norm = norm_partials[0, 0]
    norm_grad = lax.psum(local_norm, ("dp", "group"))
    grad = lax.psum_scatter(partials[0], "group", scatter_dimension=2, tiled=True)
    grad, left_root, right_root = lax.optimization_barrier((grad, left_root, right_root))
    new_moment = 0.99 * second_moment + 0.01 * grad * grad
    adam = grad / (jnp.sqrt(new_moment) + EPS_ADAM)
    adam_part = jnp.sum(adam * adam, axis=(1, 2))
    adam_sq = lax.psum(adam_part, ("dp", "group"))
    grad_low = grad.astype(jnp.bfloat16)

    mine = to_owners(grad_low)
    piece = lax.all_gather(mine, "group", axis=2, tiled=True)
    own_rows = lax.dynamic_slice_in_dim(piece, lower, quarter, 1)
    piece4 = piece.reshape(cap, n_dp, rows, width)
    gram_left = jnp.einsum("cdim,cjm->dcij", piece4, own_rows, preferred_element_type=jnp.float32)
    gram_right = jnp.einsum("cim,cij->cmj", piece, mine, preferred_element_type=jnp.float32)
    gram_right = gram_right.reshape(cap, n_dp, rows, quarter).transpose(1, 0, 2, 3)
    left_term = to_keepers(gram_left.astype(jnp.bfloat16)).astype(jnp.float32)
    right_term = to_keepers(gram_right.astype(jnp.bfloat16)).astype(jnp.float32)

    half = jnp.einsum("cim,cmj->cij", piece, right_root, preferred_element_type=jnp.float32)
    half = half.astype(jnp.bfloat16)
    full_left = lax.all_gather(left_root, "group", axis=2, tiled=True)
    full_left4 = full_left.reshape(cap, n_dp, rows, width)
    direction = jnp.einsum("cdim,cmj->dcij", full_left4, half, preferred_element_type=jnp.float32)
    direction_sq = lax.psum(jnp.sum(direction * direction, axis=(0, 2, 3)), "group")
    adam_pad = jnp.pad(adam_sq, (0, slots - count))
    adam_owned = lax.dynamic_slice_in_dim(adam_pad, me_dp * cap, cap)
    ratio = jnp.sqrt(adam_owned / (direction_sq + EPS_GRAFT))
    scaled = (ratio[None, :, None, None] * direction).astype(jnp.bfloat16)
    block_step = to_keepers(scaled)

    new_left = 0.95 * left_stats + 0.05 * left_term
    new_right = 0.95 * right_stats + 0.05 * right_term
    new_norm_moment = 0.99 * norm_moment + 0.01 * norm_grad * norm_grad
    norm_step = norm_grad / (jnp.sqrt(new_norm_moment) + EPS_ADAM)
    return (block_step, new_moment, new_left, new_right, norm_step, new_norm_moment)


def solution(mesh):
    return jax.shard_map(
        on_device,
        mesh=mesh,
        in_specs=(
            P("group", None, "dp", None),
            P(None, "dp", "group"),
            P(None, "dp", "group"),
            P(None, "dp", "group"),
            P(None, "dp", "group"),
            P(None, "dp", "group"),
            P("dp", "group", None, None),
            P(),
        ),
        out_specs=(
            P(None, "dp", "group"),
            P(None, "dp", "group"),
            P(None, "dp", "group"),
            P(None, "dp", "group"),
            P(),
            P(),
        ),
        check_vma=False,
    )
```

```python
import jax
import jax.numpy as jnp
from jax import lax
from jax.sharding import PartitionSpec as P

EPS_ADAM = 1e-08
EPS_GRAFT = 1e-06


def on_device(
    partials,
    second_moment,
    left_stats,
    right_stats,
    left_roots,
    right_roots,
    norm_partials,
    norm_moment,
):
    n_dp = lax.axis_size("dp")
    me_dp = lax.axis_index("dp")
    me_group = lax.axis_index("group")
    count = second_moment.shape[0]
    rows = partials.shape[2]
    quarter = second_moment.shape[2]
    width = rows * n_dp
    cap = -(-count // n_dp)
    slots = cap * n_dp
    lower = me_group * quarter
    split = (cap + 1) // 2
    bounds = [(0, split), (split, cap)] if cap > 1 else [(0, cap)]

    def to_owners(blocks, n_slots):
        padded = jnp.pad(blocks, ((0, n_slots * n_dp - blocks.shape[0]), (0, 0), (0, 0)))
        sent = lax.all_to_all(padded.reshape(n_slots, n_dp, rows, quarter), "dp", 1, 1, tiled=True)
        return sent.reshape(n_slots, width, quarter)

    def to_keepers(owned):
        n_slots = owned.shape[0]
        back = lax.all_to_all(owned.reshape(n_slots, n_dp, rows, quarter), "dp", 1, 1, tiled=True)
        return back.reshape(n_slots * n_dp, rows, quarter)

    left_root = to_owners(left_roots, cap)
    right_root = to_owners(right_roots, cap)
    local_norm = norm_partials[0, 0]

    moments, adam_parts, left_terms, right_terms, pieces = [], [], [], [], []
    for index, (s0, s1) in enumerate(bounds):
        b0, b1 = s0 * n_dp, min(s1 * n_dp, count)
        grad = lax.psum_scatter(partials[0, b0:b1], "group", scatter_dimension=2, tiled=True)
        if index == 0:
            grad, left_root, right_root = lax.optimization_barrier((grad, left_root, right_root))
        new_moment = 0.99 * second_moment[b0:b1] + 0.01 * grad * grad
        adam = grad / (jnp.sqrt(new_moment) + EPS_ADAM)
        adam_parts.append(jnp.sum(adam * adam, axis=(1, 2)))
        moments.append(new_moment)
        mine = to_owners(grad.astype(jnp.bfloat16), s1 - s0)
        piece = lax.all_gather(mine, "group", axis=2, tiled=True)
        own_rows = lax.dynamic_slice_in_dim(piece, lower, quarter, 1)
        gram_left = jnp.einsum("cim,cjm->cij", piece, own_rows, preferred_element_type=jnp.float32)
        gram_right = jnp.einsum("cim,cij->cmj", piece, mine, preferred_element_type=jnp.float32)
        left_terms.append(to_keepers(gram_left.astype(jnp.bfloat16))[: b1 - b0])
        right_terms.append(to_keepers(gram_right.astype(jnp.bfloat16))[: b1 - b0])
        pieces.append(piece)

    norm_grad, adam_sq = lax.psum((local_norm, jnp.concatenate(adam_parts)), ("dp", "group"))
    piece = jnp.concatenate(pieces) if len(pieces) > 1 else pieces[0]
    half = jnp.einsum("cim,cmj->cij", piece, right_root, preferred_element_type=jnp.float32)
    half = half.astype(jnp.bfloat16)
    full_left = lax.all_gather(left_root, "group", axis=2, tiled=True)
    direction = jnp.einsum("cim,cmj->cij", full_left, half, preferred_element_type=jnp.float32)
    direction_sq = lax.psum(jnp.sum(direction * direction, axis=(1, 2)), "group")
    adam_pad = jnp.pad(adam_sq, (0, slots - count)).reshape(cap, n_dp)
    adam_owned = lax.dynamic_slice_in_dim(adam_pad, me_dp, 1, 1)[:, 0]
    ratio = jnp.sqrt(adam_owned / (direction_sq + EPS_GRAFT))
    scaled = (ratio[:, None, None] * direction).astype(jnp.bfloat16)
    block_step = to_keepers(scaled)[:count]

    new_moment = jnp.concatenate(moments)
    left_term = jnp.concatenate(left_terms).astype(jnp.float32)
    right_term = jnp.concatenate(right_terms).astype(jnp.float32)
    new_left = 0.95 * left_stats + 0.05 * left_term
    new_right = 0.95 * right_stats + 0.05 * right_term
    new_norm_moment = 0.99 * norm_moment + 0.01 * norm_grad * norm_grad
    norm_step = norm_grad / (jnp.sqrt(new_norm_moment) + EPS_ADAM)
    return (block_step, new_moment, new_left, new_right, norm_step, new_norm_moment)


def solution(mesh):
    return jax.shard_map(
        on_device,
        mesh=mesh,
        in_specs=(
            P("group", None, "dp", None),
            P(None, "dp", "group"),
            P(None, "dp", "group"),
            P(None, "dp", "group"),
            P(None, "dp", "group"),
            P(None, "dp", "group"),
            P("dp", "group", None, None),
            P(),
        ),
        out_specs=(
            P(None, "dp", "group"),
            P(None, "dp", "group"),
            P(None, "dp", "group"),
            P(None, "dp", "group"),
            P(),
            P(),
        ),
        check_vma=False,
    )
```

```python
import jax
import jax.numpy as jnp
from jax import lax
from jax.sharding import PartitionSpec as P

EPS_ADAM = 1e-08
EPS_GRAFT = 1e-06


def on_device(
    partials,
    second_moment,
    left_stats,
    right_stats,
    left_roots,
    right_roots,
    norm_partials,
    norm_moment,
):
    n_dp = lax.axis_size("dp")
    me_dp = lax.axis_index("dp")
    me_group = lax.axis_index("group")
    count = second_moment.shape[0]
    rows = partials.shape[2]
    quarter = second_moment.shape[2]
    width = rows * n_dp
    cap = -(-count // n_dp)
    slots = cap * n_dp
    lower = me_group * quarter
    split = (cap + 1) // 2
    bounds = [(0, split), (split, cap)] if cap > 1 else [(0, cap)]

    def to_owners(blocks, n_slots):
        padded = jnp.pad(blocks, ((0, n_slots * n_dp - blocks.shape[0]), (0, 0), (0, 0)))
        sent = lax.all_to_all(padded.reshape(n_slots, n_dp, rows, quarter), "dp", 1, 1, tiled=True)
        return sent.reshape(n_slots, width, quarter)

    def to_keepers(owned):
        n_slots = owned.shape[0]
        back = lax.all_to_all(owned.reshape(n_slots, n_dp, rows, quarter), "dp", 1, 1, tiled=True)
        return back.reshape(n_slots * n_dp, rows, quarter)

    left_root = to_owners(left_roots, cap)
    right_root = to_owners(right_roots, cap)
    local_norm = norm_partials[0, 0]

    moments, adam_parts, left_terms, right_terms, pieces = [], [], [], [], []
    for index, (s0, s1) in enumerate(bounds):
        b0, b1 = s0 * n_dp, min(s1 * n_dp, count)
        grad = lax.psum_scatter(partials[0, b0:b1], "group", scatter_dimension=2, tiled=True)
        if index == 0:
            grad, left_root, right_root = lax.optimization_barrier((grad, left_root, right_root))
        new_moment = 0.99 * second_moment[b0:b1] + 0.01 * grad * grad
        adam = grad / (jnp.sqrt(new_moment) + EPS_ADAM)
        adam_parts.append(jnp.sum(adam * adam, axis=(1, 2)))
        moments.append(new_moment)
        mine = to_owners(grad.astype(jnp.bfloat16), s1 - s0)
        piece = lax.all_gather(mine, "group", axis=2, tiled=True)
        own_rows = lax.dynamic_slice_in_dim(piece, lower, quarter, 1)
        gram_left = jnp.einsum("cim,cjm->cij", piece, own_rows, preferred_element_type=jnp.float32)
        gram_right = jnp.einsum("cim,cij->cmj", piece, mine, preferred_element_type=jnp.float32)
        left_terms.append(to_keepers(gram_left.astype(jnp.bfloat16))[: b1 - b0])
        right_terms.append(to_keepers(gram_right.astype(jnp.bfloat16))[: b1 - b0])
        pieces.append(piece)

    piece = jnp.concatenate(pieces) if len(pieces) > 1 else pieces[0]
    half = jnp.einsum("cim,cmj->cij", piece, right_root, preferred_element_type=jnp.float32)
    half = half.astype(jnp.bfloat16)
    full_left = lax.all_gather(left_root, "group", axis=2, tiled=True)
    direction = jnp.einsum("cim,cmj->cij", full_left, half, preferred_element_type=jnp.float32)
    direction_part = jnp.sum(direction * direction, axis=(1, 2))
    direction_rows = lax.dynamic_update_slice_in_dim(
        jnp.zeros((n_dp, cap), jnp.float32), direction_part[None], me_dp, 0
    )
    sums, left_terms, right_terms = lax.optimization_barrier(
        ((local_norm, jnp.concatenate(adam_parts), direction_rows), left_terms, right_terms)
    )
    norm_grad, adam_sq, direction_all = lax.psum(sums, ("dp", "group"))
    direction_sq = lax.dynamic_slice_in_dim(direction_all, me_dp, 1, 0)[0]
    adam_pad = jnp.pad(adam_sq, (0, slots - count)).reshape(cap, n_dp)
    adam_owned = lax.dynamic_slice_in_dim(adam_pad, me_dp, 1, 1)[:, 0]
    ratio = jnp.sqrt(adam_owned / (direction_sq + EPS_GRAFT))
    scaled = (ratio[:, None, None] * direction).astype(jnp.bfloat16)
    block_step = to_keepers(scaled)[:count]

    new_moment = jnp.concatenate(moments)
    left_term = jnp.concatenate(left_terms).astype(jnp.float32)
    right_term = jnp.concatenate(right_terms).astype(jnp.float32)
    new_left = 0.95 * left_stats + 0.05 * left_term
    new_right = 0.95 * right_stats + 0.05 * right_term
    new_norm_moment = 0.99 * norm_moment + 0.01 * norm_grad * norm_grad
    norm_step = norm_grad / (jnp.sqrt(new_norm_moment) + EPS_ADAM)
    return (block_step, new_moment, new_left, new_right, norm_step, new_norm_moment)


def solution(mesh):
    return jax.shard_map(
        on_device,
        mesh=mesh,
        in_specs=(
            P("group", None, "dp", None),
            P(None, "dp", "group"),
            P(None, "dp", "group"),
            P(None, "dp", "group"),
            P(None, "dp", "group"),
            P(None, "dp", "group"),
            P("dp", "group", None, None),
            P(),
        ),
        out_specs=(
            P(None, "dp", "group"),
            P(None, "dp", "group"),
            P(None, "dp", "group"),
            P(None, "dp", "group"),
            P(),
            P(),
        ),
        check_vma=False,
    )
```

```python
import jax
import jax.numpy as jnp
from jax import lax
from jax.sharding import PartitionSpec as P

EPS_ADAM = 1e-08
EPS_GRAFT = 1e-06


def on_device(
    partials,
    second_moment,
    left_stats,
    right_stats,
    left_roots,
    right_roots,
    norm_partials,
    norm_moment,
):
    n_dp = lax.axis_size("dp")
    me_dp = lax.axis_index("dp")
    me_group = lax.axis_index("group")
    count = second_moment.shape[0]
    rows = partials.shape[2]
    quarter = second_moment.shape[2]
    width = rows * n_dp
    cap = -(-count // n_dp)
    slots = cap * n_dp
    lower = me_group * quarter
    split = (cap + 1) // 2
    bounds = [(0, split), (split, cap)] if cap > 1 else [(0, cap)]

    def to_owners(blocks, n_slots):
        padded = jnp.pad(blocks, ((0, n_slots * n_dp - blocks.shape[0]), (0, 0), (0, 0)))
        sent = lax.all_to_all(padded.reshape(n_slots, n_dp, rows, quarter), "dp", 1, 1, tiled=True)
        return sent.reshape(n_slots, width, quarter)

    def to_keepers(owned):
        n_slots = owned.shape[0]
        back = lax.all_to_all(owned.reshape(n_slots, n_dp, rows, quarter), "dp", 1, 1, tiled=True)
        return back.reshape(n_slots * n_dp, rows, quarter)

    left_root = to_owners(left_roots, cap)
    right_root = to_owners(right_roots, cap)
    local_norm = norm_partials[0, 0]

    moments, adam_parts, left_terms, right_terms, pieces = [], [], [], [], []
    for index, (s0, s1) in enumerate(bounds):
        b0, b1 = s0 * n_dp, min(s1 * n_dp, count)
        grad = lax.psum_scatter(partials[0, b0:b1], "group", scatter_dimension=2, tiled=True)
        if index == 0:
            grad, left_root, right_root = lax.optimization_barrier((grad, left_root, right_root))
        new_moment = 0.99 * second_moment[b0:b1] + 0.01 * grad * grad
        adam = grad / (jnp.sqrt(new_moment) + EPS_ADAM)
        adam_parts.append(jnp.sum(adam * adam, axis=(1, 2)))
        moments.append(new_moment)
        mine = to_owners(grad.astype(jnp.bfloat16), s1 - s0)
        piece = lax.all_gather(mine, "group", axis=2, tiled=True)
        own_rows = lax.dynamic_slice_in_dim(piece, lower, quarter, 1)
        gram_left = jnp.einsum("cim,cjm->cij", piece, own_rows, preferred_element_type=jnp.float32)
        gram_right = jnp.einsum("cim,cij->cmj", piece, mine, preferred_element_type=jnp.float32)
        left_terms.append(to_keepers(gram_left.astype(jnp.bfloat16))[: b1 - b0])
        right_terms.append(to_keepers(gram_right.astype(jnp.bfloat16))[: b1 - b0])
        pieces.append(piece)

    flat = jnp.concatenate([local_norm.reshape(-1)] + adam_parts)
    total = lax.psum(jnp.pad(flat, (0, max(16384 - flat.shape[0], 0))), ("dp", "group"))
    norm_grad = total[: local_norm.size].reshape(local_norm.shape)
    adam_sq = total[local_norm.size : local_norm.size + count]
    piece = jnp.concatenate(pieces) if len(pieces) > 1 else pieces[0]
    half = jnp.einsum("cim,cmj->cij", piece, right_root, preferred_element_type=jnp.float32)
    half = half.astype(jnp.bfloat16)
    full_left = lax.all_gather(left_root, "group", axis=2, tiled=True)
    direction = jnp.einsum("cim,cmj->cij", full_left, half, preferred_element_type=jnp.float32)
    direction_sq = lax.psum(jnp.sum(direction * direction, axis=(1, 2)), "group")
    adam_pad = jnp.pad(adam_sq, (0, slots - count)).reshape(cap, n_dp)
    adam_owned = lax.dynamic_slice_in_dim(adam_pad, me_dp, 1, 1)[:, 0]
    ratio = jnp.sqrt(adam_owned / (direction_sq + EPS_GRAFT))
    scaled = (ratio[:, None, None] * direction).astype(jnp.bfloat16)
    block_step = to_keepers(scaled)[:count]

    new_moment = jnp.concatenate(moments)
    left_term = jnp.concatenate(left_terms).astype(jnp.float32)
    right_term = jnp.concatenate(right_terms).astype(jnp.float32)
    new_left = 0.95 * left_stats + 0.05 * left_term
    new_right = 0.95 * right_stats + 0.05 * right_term
    new_norm_moment = 0.99 * norm_moment + 0.01 * norm_grad * norm_grad
    norm_step = norm_grad / (jnp.sqrt(new_norm_moment) + EPS_ADAM)
    return (block_step, new_moment, new_left, new_right, norm_step, new_norm_moment)


def solution(mesh):
    return jax.shard_map(
        on_device,
        mesh=mesh,
        in_specs=(
            P("group", None, "dp", None),
            P(None, "dp", "group"),
            P(None, "dp", "group"),
            P(None, "dp", "group"),
            P(None, "dp", "group"),
            P(None, "dp", "group"),
            P("dp", "group", None, None),
            P(),
        ),
        out_specs=(
            P(None, "dp", "group"),
            P(None, "dp", "group"),
            P(None, "dp", "group"),
            P(None, "dp", "group"),
            P(),
            P(),
        ),
        check_vma=False,
    )
```

```python
import jax
import jax.numpy as jnp
from jax import lax
from jax.sharding import PartitionSpec as P

EPS_ADAM = 1e-08
EPS_GRAFT = 1e-06


def on_device(
    partials,
    second_moment,
    left_stats,
    right_stats,
    left_roots,
    right_roots,
    norm_partials,
    norm_moment,
):
    n_dp = lax.axis_size("dp")
    me_dp = lax.axis_index("dp")
    me_group = lax.axis_index("group")
    count = second_moment.shape[0]
    rows = partials.shape[2]
    quarter = second_moment.shape[2]
    width = rows * n_dp
    cap = -(-count // n_dp)
    slots = cap * n_dp
    lower = me_group * quarter
    split = (cap + 1) // 2
    bounds = [(0, split), (split, cap)] if cap > 1 else [(0, cap)]

    def to_owners(blocks, n_slots):
        padded = jnp.pad(blocks, ((0, n_slots * n_dp - blocks.shape[0]), (0, 0), (0, 0)))
        sent = lax.all_to_all(padded.reshape(n_slots, n_dp, rows, quarter), "dp", 1, 1, tiled=True)
        return sent.reshape(n_slots, width, quarter)

    def to_keepers(owned):
        n_slots = owned.shape[0]
        back = lax.all_to_all(owned.reshape(n_slots, n_dp, rows, quarter), "dp", 1, 1, tiled=True)
        return back.reshape(n_slots * n_dp, rows, quarter)

    left_root = to_owners(left_roots, cap)
    right_root = to_owners(right_roots, cap)
    local_norm = norm_partials[0, 0]

    grads, moments, adam_parts = [], [], []
    for index, (s0, s1) in enumerate(bounds):
        b0, b1 = s0 * n_dp, min(s1 * n_dp, count)
        grad = lax.psum_scatter(partials[0, b0:b1], "group", scatter_dimension=2, tiled=True)
        if index == 0:
            grad, left_root, right_root = lax.optimization_barrier((grad, left_root, right_root))
        new_moment = 0.99 * second_moment[b0:b1] + 0.01 * grad * grad
        adam = grad / (jnp.sqrt(new_moment) + EPS_ADAM)
        adam_parts.append(jnp.sum(adam * adam, axis=(1, 2)))
        moments.append(new_moment)
        grads.append(grad.astype(jnp.bfloat16))

    norm_grad, adam_sq = lax.psum((local_norm, jnp.concatenate(adam_parts)), ("dp", "group"))
    norm_grad, adam_sq, grads[0] = lax.optimization_barrier((norm_grad, adam_sq, grads[0]))

    left_terms, right_terms, pieces = [], [], []
    for (s0, s1), grad_low in zip(bounds, grads):
        b0, b1 = s0 * n_dp, min(s1 * n_dp, count)
        mine = to_owners(grad_low, s1 - s0)
        piece = lax.all_gather(mine, "group", axis=2, tiled=True)
        own_rows = lax.dynamic_slice_in_dim(piece, lower, quarter, 1)
        gram_left = jnp.einsum("cim,cjm->cij", piece, own_rows, preferred_element_type=jnp.float32)
        gram_right = jnp.einsum("cim,cij->cmj", piece, mine, preferred_element_type=jnp.float32)
        left_terms.append(to_keepers(gram_left.astype(jnp.bfloat16))[: b1 - b0])
        right_terms.append(to_keepers(gram_right.astype(jnp.bfloat16))[: b1 - b0])
        pieces.append(piece)

    piece = jnp.concatenate(pieces) if len(pieces) > 1 else pieces[0]
    half = jnp.einsum("cim,cmj->cij", piece, right_root, preferred_element_type=jnp.float32)
    half = half.astype(jnp.bfloat16)
    full_left = lax.all_gather(left_root, "group", axis=2, tiled=True)
    direction = jnp.einsum("cim,cmj->cij", full_left, half, preferred_element_type=jnp.float32)
    direction_sq = lax.psum(jnp.sum(direction * direction, axis=(1, 2)), "group")
    adam_pad = jnp.pad(adam_sq, (0, slots - count)).reshape(cap, n_dp)
    adam_owned = lax.dynamic_slice_in_dim(adam_pad, me_dp, 1, 1)[:, 0]
    ratio = jnp.sqrt(adam_owned / (direction_sq + EPS_GRAFT))
    scaled = (ratio[:, None, None] * direction).astype(jnp.bfloat16)
    block_step = to_keepers(scaled)[:count]

    new_moment = jnp.concatenate(moments)
    left_term = jnp.concatenate(left_terms).astype(jnp.float32)
    right_term = jnp.concatenate(right_terms).astype(jnp.float32)
    new_left = 0.95 * left_stats + 0.05 * left_term
    new_right = 0.95 * right_stats + 0.05 * right_term
    new_norm_moment = 0.99 * norm_moment + 0.01 * norm_grad * norm_grad
    norm_step = norm_grad / (jnp.sqrt(new_norm_moment) + EPS_ADAM)
    return (block_step, new_moment, new_left, new_right, norm_step, new_norm_moment)


def solution(mesh):
    return jax.shard_map(
        on_device,
        mesh=mesh,
        in_specs=(
            P("group", None, "dp", None),
            P(None, "dp", "group"),
            P(None, "dp", "group"),
            P(None, "dp", "group"),
            P(None, "dp", "group"),
            P(None, "dp", "group"),
            P("dp", "group", None, None),
            P(),
        ),
        out_specs=(
            P(None, "dp", "group"),
            P(None, "dp", "group"),
            P(None, "dp", "group"),
            P(None, "dp", "group"),
            P(),
            P(),
        ),
        check_vma=False,
    )
```

```python
import jax
import jax.numpy as jnp
from jax import lax
from jax.sharding import PartitionSpec as P

EPS_ADAM = 1e-08
EPS_GRAFT = 1e-06


def on_device(
    partials,
    second_moment,
    left_stats,
    right_stats,
    left_roots,
    right_roots,
    norm_partials,
    norm_moment,
):
    n_dp = lax.axis_size("dp")
    me_dp = lax.axis_index("dp")
    me_group = lax.axis_index("group")
    count = second_moment.shape[0]
    rows = partials.shape[2]
    quarter = second_moment.shape[2]
    width = rows * n_dp
    cap = -(-count // n_dp)
    slots = cap * n_dp
    lower = me_group * quarter
    split = (cap + 1) // 2
    bounds = [(0, split), (split, cap)] if cap > 1 else [(0, cap)]

    def to_owners(blocks, n_slots):
        padded = jnp.pad(blocks, ((0, n_slots * n_dp - blocks.shape[0]), (0, 0), (0, 0)))
        sent = lax.all_to_all(padded.reshape(n_slots, n_dp, rows, quarter), "dp", 1, 1, tiled=True)
        return sent.reshape(n_slots, width, quarter)

    def to_keepers(owned):
        n_slots = owned.shape[0]
        back = lax.all_to_all(owned.reshape(n_slots, n_dp, rows, quarter), "dp", 1, 1, tiled=True)
        return back.reshape(n_slots * n_dp, rows, quarter)

    left_root = to_owners(left_roots, cap)
    right_root = to_owners(right_roots, cap)
    local_norm = norm_partials[0, 0]

    grads, moments, adam_parts = [], [], []
    for index, (s0, s1) in enumerate(bounds):
        b0, b1 = s0 * n_dp, min(s1 * n_dp, count)
        grad = lax.psum_scatter(partials[0, b0:b1], "group", scatter_dimension=2, tiled=True)
        if index == 0:
            grad, left_root, right_root = lax.optimization_barrier((grad, left_root, right_root))
        new_moment = 0.99 * second_moment[b0:b1] + 0.01 * grad * grad
        adam = grad / (jnp.sqrt(new_moment) + EPS_ADAM)
        adam_parts.append(jnp.sum(adam * adam, axis=(1, 2)))
        moments.append(new_moment)
        grads.append(grad.astype(jnp.bfloat16))

    adam_cat = jnp.pad(jnp.concatenate(adam_parts), (0, slots - count))
    adam_rows = adam_cat.reshape(cap, n_dp).T
    norm_rows = jnp.broadcast_to(local_norm.reshape(1, -1), (n_dp, local_norm.size))
    sent = lax.all_to_all(jnp.concatenate([adam_rows, norm_rows], axis=1), "dp", 0, 0, tiled=True)
    dp_sums = jnp.sum(sent, axis=0)
    dp_sums, grads[0] = lax.optimization_barrier((dp_sums, grads[0]))

    left_terms, right_terms, pieces = [], [], []
    for (s0, s1), grad_low in zip(bounds, grads):
        b0, b1 = s0 * n_dp, min(s1 * n_dp, count)
        mine = to_owners(grad_low, s1 - s0)
        piece = lax.all_gather(mine, "group", axis=2, tiled=True)
        own_rows = lax.dynamic_slice_in_dim(piece, lower, quarter, 1)
        gram_left = jnp.einsum("cim,cjm->cij", piece, own_rows, preferred_element_type=jnp.float32)
        gram_right = jnp.einsum("cim,cij->cmj", piece, mine, preferred_element_type=jnp.float32)
        left_terms.append(to_keepers(gram_left.astype(jnp.bfloat16))[: b1 - b0])
        right_terms.append(to_keepers(gram_right.astype(jnp.bfloat16))[: b1 - b0])
        pieces.append(piece)

    piece = jnp.concatenate(pieces) if len(pieces) > 1 else pieces[0]
    half = jnp.einsum("cim,cmj->cij", piece, right_root, preferred_element_type=jnp.float32)
    half = half.astype(jnp.bfloat16)
    full_left = lax.all_gather(left_root, "group", axis=2, tiled=True)
    direction = jnp.einsum("cim,cmj->cij", full_left, half, preferred_element_type=jnp.float32)
    totals = lax.psum(jnp.concatenate([jnp.sum(direction * direction, axis=(1, 2)), dp_sums]), "group")
    direction_sq = totals[:cap]
    adam_owned = totals[cap : 2 * cap]
    norm_grad = totals[2 * cap :].reshape(local_norm.shape)
    ratio = jnp.sqrt(adam_owned / (direction_sq + EPS_GRAFT))
    scaled = (ratio[:, None, None] * direction).astype(jnp.bfloat16)
    block_step = to_keepers(scaled)[:count]

    new_moment = jnp.concatenate(moments)
    left_term = jnp.concatenate(left_terms).astype(jnp.float32)
    right_term = jnp.concatenate(right_terms).astype(jnp.float32)
    new_left = 0.95 * left_stats + 0.05 * left_term
    new_right = 0.95 * right_stats + 0.05 * right_term
    new_norm_moment = 0.99 * norm_moment + 0.01 * norm_grad * norm_grad
    norm_step = norm_grad / (jnp.sqrt(new_norm_moment) + EPS_ADAM)
    return (block_step, new_moment, new_left, new_right, norm_step, new_norm_moment)


def solution(mesh):
    return jax.shard_map(
        on_device,
        mesh=mesh,
        in_specs=(
            P("group", None, "dp", None),
            P(None, "dp", "group"),
            P(None, "dp", "group"),
            P(None, "dp", "group"),
            P(None, "dp", "group"),
            P(None, "dp", "group"),
            P("dp", "group", None, None),
            P(),
        ),
        out_specs=(
            P(None, "dp", "group"),
            P(None, "dp", "group"),
            P(None, "dp", "group"),
            P(None, "dp", "group"),
            P(),
            P(),
        ),
        check_vma=False,
    )
```

```python
import jax
import jax.numpy as jnp
from jax import lax
from jax.sharding import PartitionSpec as P

EPS_ADAM = 1e-08
EPS_GRAFT = 1e-06


def on_device(
    partials,
    second_moment,
    left_stats,
    right_stats,
    left_roots,
    right_roots,
    norm_partials,
    norm_moment,
):
    n_dp = lax.axis_size("dp")
    me_dp = lax.axis_index("dp")
    me_group = lax.axis_index("group")
    count = second_moment.shape[0]
    rows = partials.shape[2]
    quarter = second_moment.shape[2]
    width = rows * n_dp
    cap = -(-count // n_dp)
    slots = cap * n_dp
    lower = me_group * quarter
    split = (cap + 1) // 2
    bounds = [(0, split), (split, cap)] if cap > 1 else [(0, cap)]

    def pad_slots(blocks, n_slots):
        return jnp.pad(blocks, ((0, n_slots * n_dp - blocks.shape[0]), (0, 0), (0, 0)))

    def to_owners(blocks, n_slots):
        padded = pad_slots(blocks, n_slots)
        sent = lax.all_to_all(padded.reshape(n_slots, n_dp, rows, quarter), "dp", 1, 1, tiled=True)
        return sent.reshape(n_slots, width, quarter)

    def gather_columns(mine):
        n_group = lax.axis_size("group")
        spread = jnp.broadcast_to(mine[None], (n_group,) + mine.shape)
        got = lax.all_to_all(spread, "group", 0, 0, tiled=True)
        return got.transpose(1, 2, 0, 3).reshape(mine.shape[0], width, n_group * quarter)

    def to_keepers(owned):
        n_slots = owned.shape[0]
        back = lax.all_to_all(owned.reshape(n_slots, n_dp, rows, quarter), "dp", 1, 1, tiled=True)
        return back.reshape(n_slots * n_dp, rows, quarter)

    left_root = to_owners(left_roots, cap)
    right_root = to_owners(right_roots, cap)
    local_norm = norm_partials[0, 0]

    def chunk_grad(s0, s1):
        b0, b1 = s0 * n_dp, min(s1 * n_dp, count)
        return lax.psum_scatter(partials[0, b0:b1], "group", scatter_dimension=2, tiled=True)

    def chunk_terms(grad, s0, s1):
        b0, b1 = s0 * n_dp, min(s1 * n_dp, count)
        new_moment = 0.99 * second_moment[b0:b1] + 0.01 * grad * grad
        adam = grad / (jnp.sqrt(new_moment) + EPS_ADAM)
        return new_moment, jnp.sum(adam * adam, axis=(1, 2)), grad.astype(jnp.bfloat16)

    def chunk_grams(piece, mine, s0, s1):
        b0, b1 = s0 * n_dp, min(s1 * n_dp, count)
        own_rows = lax.dynamic_slice_in_dim(piece, lower, quarter, 1)
        gram_left = jnp.einsum("cim,cjm->cij", piece, own_rows, preferred_element_type=jnp.float32)
        gram_right = jnp.einsum("cim,cij->cmj", piece, mine, preferred_element_type=jnp.float32)
        left = to_keepers(gram_left.astype(jnp.bfloat16))[: b1 - b0]
        right = to_keepers(gram_right.astype(jnp.bfloat16))[: b1 - b0]
        return left, right

    (a0, a1) = bounds[0]
    if len(bounds) > 1:
        (c0, c1) = bounds[1]
        moment_b, adam_b, low_b = chunk_terms(chunk_grad(c0, c1), c0, c1)
        mine_b = to_owners(low_b, c1 - c0)
        piece_b = gather_columns(mine_b)
        grad_a = chunk_grad(a0, a1)
        grad_a, left_root, right_root, piece_b = lax.optimization_barrier((grad_a, left_root, right_root, piece_b))
    else:
        grad_a = chunk_grad(a0, a1)
        grad_a, left_root, right_root = lax.optimization_barrier((grad_a, left_root, right_root))
    moment_a, adam_a, low_a = chunk_terms(grad_a, a0, a1)
    moments, adam_parts = [moment_a], [adam_a]
    if len(bounds) > 1:
        moments.append(moment_b)
        adam_parts.append(adam_b)

    adam_cat = jnp.pad(jnp.concatenate(adam_parts), (0, slots - count))
    adam_rows = adam_cat.reshape(cap, n_dp).T
    norm_rows = jnp.broadcast_to(local_norm.reshape(1, -1), (n_dp, local_norm.size))
    sent = lax.all_to_all(jnp.concatenate([adam_rows, norm_rows], axis=1), "dp", 0, 0, tiled=True)
    dp_sums = jnp.sum(sent, axis=0)
    dp_sums, low_a = lax.optimization_barrier((dp_sums, low_a))

    mine_a = to_owners(low_a, a1 - a0)
    piece_a = lax.all_gather(mine_a, "group", axis=2, tiled=True)
    left_a, right_a = chunk_grams(piece_a, mine_a, a0, a1)
    pieces, left_terms, right_terms = [piece_a], [left_a], [right_a]
    if len(bounds) > 1:
        left_b, right_b = chunk_grams(piece_b, mine_b, c0, c1)
        pieces.append(piece_b)
        left_terms.append(left_b)
        right_terms.append(right_b)

    piece = jnp.concatenate(pieces) if len(pieces) > 1 else pieces[0]
    half = jnp.einsum("cim,cmj->cij", piece, right_root, preferred_element_type=jnp.float32)
    half = half.astype(jnp.bfloat16)
    full_left = lax.all_gather(left_root, "group", axis=2, tiled=True)
    direction = jnp.einsum("cim,cmj->cij", full_left, half, preferred_element_type=jnp.float32)
    totals = lax.psum(jnp.concatenate([jnp.sum(direction * direction, axis=(1, 2)), dp_sums[:cap]]), "group")
    direction_sq = totals[:cap]
    adam_owned = totals[cap:]
    ratio = jnp.sqrt(adam_owned / (direction_sq + EPS_GRAFT))
    scaled = (ratio[:, None, None] * direction).astype(jnp.bfloat16)
    scaled, norm_dp = lax.optimization_barrier((scaled, dp_sums[cap:]))
    block_step = to_keepers(scaled)[:count]
    norm_grad = lax.psum(norm_dp, "group").reshape(local_norm.shape)

    new_moment = jnp.concatenate(moments)
    left_term = jnp.concatenate(left_terms).astype(jnp.float32)
    right_term = jnp.concatenate(right_terms).astype(jnp.float32)
    new_left = 0.95 * left_stats + 0.05 * left_term
    new_right = 0.95 * right_stats + 0.05 * right_term
    new_norm_moment = 0.99 * norm_moment + 0.01 * norm_grad * norm_grad
    norm_step = norm_grad / (jnp.sqrt(new_norm_moment) + EPS_ADAM)
    return (block_step, new_moment, new_left, new_right, norm_step, new_norm_moment)


def solution(mesh):
    return jax.shard_map(
        on_device,
        mesh=mesh,
        in_specs=(
            P("group", None, "dp", None),
            P(None, "dp", "group"),
            P(None, "dp", "group"),
            P(None, "dp", "group"),
            P(None, "dp", "group"),
            P(None, "dp", "group"),
            P("dp", "group", None, None),
            P(),
        ),
        out_specs=(
            P(None, "dp", "group"),
            P(None, "dp", "group"),
            P(None, "dp", "group"),
            P(None, "dp", "group"),
            P(),
            P(),
        ),
        check_vma=False,
    )
```

```python
import jax
import jax.numpy as jnp
from jax import lax
from jax.sharding import PartitionSpec as P

EPS_ADAM = 1e-08
EPS_GRAFT = 1e-06


def on_device(
    partials,
    second_moment,
    left_stats,
    right_stats,
    left_roots,
    right_roots,
    norm_partials,
    norm_moment,
):
    n_dp = lax.axis_size("dp")
    me_dp = lax.axis_index("dp")
    me_group = lax.axis_index("group")
    count = second_moment.shape[0]
    rows = partials.shape[2]
    quarter = second_moment.shape[2]
    width = rows * n_dp
    cap = -(-count // n_dp)
    slots = cap * n_dp
    lower = me_group * quarter
    split = (cap + 1) // 2
    bounds = [(0, split), (split, cap)] if cap > 1 else [(0, cap)]

    def to_owners(blocks, n_slots):
        padded = jnp.pad(blocks, ((0, n_slots * n_dp - blocks.shape[0]), (0, 0), (0, 0)))
        sent = lax.all_to_all(padded.reshape(n_slots, n_dp, rows, quarter), "dp", 1, 1, tiled=True)
        return sent.reshape(n_slots, width, quarter)

    def to_keepers(owned):
        n_slots = owned.shape[0]
        back = lax.all_to_all(owned.reshape(n_slots, n_dp, rows, quarter), "dp", 1, 1, tiled=True)
        return back.reshape(n_slots * n_dp, rows, quarter)

    left_root = to_owners(left_roots, cap)
    right_root = to_owners(right_roots, cap)
    local_norm = norm_partials[0, 0]

    grads, moments, adam_parts = [], [], []
    for index, (s0, s1) in enumerate(bounds):
        b0, b1 = s0 * n_dp, min(s1 * n_dp, count)
        grad = lax.psum_scatter(partials[0, b0:b1], "group", scatter_dimension=2, tiled=True)
        if index == 0:
            grad, left_root, right_root = lax.optimization_barrier((grad, left_root, right_root))
        new_moment = 0.99 * second_moment[b0:b1] + 0.01 * grad * grad
        adam = grad / (jnp.sqrt(new_moment) + EPS_ADAM)
        adam_parts.append(jnp.sum(adam * adam, axis=(1, 2)))
        moments.append(new_moment)
        grads.append(grad.astype(jnp.bfloat16))

    adam_cat = jnp.pad(jnp.concatenate(adam_parts), (0, slots - count))
    adam_rows = adam_cat.reshape(cap, n_dp).T
    norm_rows = jnp.broadcast_to(local_norm.reshape(1, -1), (n_dp, local_norm.size))
    sent = lax.all_to_all(jnp.concatenate([adam_rows, norm_rows], axis=1), "dp", 0, 0, tiled=True)
    dp_sums = jnp.sum(sent, axis=0)

    left_terms, right_terms, pieces = [], [], []
    for (s0, s1), grad_low in zip(bounds, grads):
        b0, b1 = s0 * n_dp, min(s1 * n_dp, count)
        mine = to_owners(grad_low, s1 - s0)
        piece = lax.all_gather(mine, "group", axis=2, tiled=True)
        if s0 == 0:
            dp_sums, piece = lax.optimization_barrier((dp_sums, piece))
        own_rows = lax.dynamic_slice_in_dim(piece, lower, quarter, 1)
        gram_left = jnp.einsum("cim,cjm->cij", piece, own_rows, preferred_element_type=jnp.float32)
        gram_right = jnp.einsum("cim,cij->cmj", piece, mine, preferred_element_type=jnp.float32)
        left_terms.append(to_keepers(gram_left.astype(jnp.bfloat16))[: b1 - b0])
        right_terms.append(to_keepers(gram_right.astype(jnp.bfloat16))[: b1 - b0])
        pieces.append(piece)

    piece = jnp.concatenate(pieces) if len(pieces) > 1 else pieces[0]
    half = jnp.einsum("cim,cmj->cij", piece, right_root, preferred_element_type=jnp.float32)
    half = half.astype(jnp.bfloat16)
    full_left = lax.all_gather(left_root, "group", axis=2, tiled=True)
    direction = jnp.einsum("cim,cmj->cij", full_left, half, preferred_element_type=jnp.float32)
    totals = lax.psum(jnp.concatenate([jnp.sum(direction * direction, axis=(1, 2)), dp_sums[:cap]]), "group")
    direction_sq = totals[:cap]
    adam_owned = totals[cap:]
    ratio = jnp.sqrt(adam_owned / (direction_sq + EPS_GRAFT))
    scaled = (ratio[:, None, None] * direction).astype(jnp.bfloat16)
    scaled, norm_dp = lax.optimization_barrier((scaled, dp_sums[cap:]))
    block_step = to_keepers(scaled)[:count]
    norm_grad = lax.psum(norm_dp, "group").reshape(local_norm.shape)

    new_moment = jnp.concatenate(moments)
    left_term = jnp.concatenate(left_terms).astype(jnp.float32)
    right_term = jnp.concatenate(right_terms).astype(jnp.float32)
    new_left = 0.95 * left_stats + 0.05 * left_term
    new_right = 0.95 * right_stats + 0.05 * right_term
    new_norm_moment = 0.99 * norm_moment + 0.01 * norm_grad * norm_grad
    norm_step = norm_grad / (jnp.sqrt(new_norm_moment) + EPS_ADAM)
    return (block_step, new_moment, new_left, new_right, norm_step, new_norm_moment)


def solution(mesh):
    return jax.shard_map(
        on_device,
        mesh=mesh,
        in_specs=(
            P("group", None, "dp", None),
            P(None, "dp", "group"),
            P(None, "dp", "group"),
            P(None, "dp", "group"),
            P(None, "dp", "group"),
            P(None, "dp", "group"),
            P("dp", "group", None, None),
            P(),
        ),
        out_specs=(
            P(None, "dp", "group"),
            P(None, "dp", "group"),
            P(None, "dp", "group"),
            P(None, "dp", "group"),
            P(),
            P(),
        ),
        check_vma=False,
    )
```

```python
import jax
import jax.numpy as jnp
from jax import lax
from jax.sharding import PartitionSpec as P

EPS_ADAM = 1e-08
EPS_GRAFT = 1e-06


def on_device(
    partials,
    second_moment,
    left_stats,
    right_stats,
    left_roots,
    right_roots,
    norm_partials,
    norm_moment,
):
    n_dp = lax.axis_size("dp")
    me_dp = lax.axis_index("dp")
    me_group = lax.axis_index("group")
    count = second_moment.shape[0]
    rows = partials.shape[2]
    quarter = second_moment.shape[2]
    width = rows * n_dp
    cap = -(-count // n_dp)
    slots = cap * n_dp
    lower = me_group * quarter
    split = cap // 2
    bounds = [(0, split), (split, cap)] if cap > 1 else [(0, cap)]

    def to_owners(blocks, n_slots):
        padded = jnp.pad(blocks, ((0, n_slots * n_dp - blocks.shape[0]), (0, 0), (0, 0)))
        sent = lax.all_to_all(padded.reshape(n_slots, n_dp, rows, quarter), "dp", 1, 1, tiled=True)
        return sent.reshape(n_slots, width, quarter)

    def to_keepers(owned):
        n_slots = owned.shape[0]
        back = lax.all_to_all(owned.reshape(n_slots, n_dp, rows, quarter), "dp", 1, 1, tiled=True)
        return back.reshape(n_slots * n_dp, rows, quarter)

    left_root = to_owners(left_roots, cap)
    right_root = to_owners(right_roots, cap)
    local_norm = norm_partials[0, 0]

    grads, moments, adam_parts = [], [], []
    for index, (s0, s1) in enumerate(bounds):
        b0, b1 = s0 * n_dp, min(s1 * n_dp, count)
        grad = lax.psum_scatter(partials[0, b0:b1], "group", scatter_dimension=2, tiled=True)
        if index == 0:
            grad, left_root, right_root = lax.optimization_barrier((grad, left_root, right_root))
        new_moment = 0.99 * second_moment[b0:b1] + 0.01 * grad * grad
        adam = grad / (jnp.sqrt(new_moment) + EPS_ADAM)
        adam_parts.append(jnp.sum(adam * adam, axis=(1, 2)))
        moments.append(new_moment)
        grads.append(grad.astype(jnp.bfloat16))

    adam_cat = jnp.pad(jnp.concatenate(adam_parts), (0, slots - count))
    adam_rows = adam_cat.reshape(cap, n_dp).T
    norm_rows = jnp.broadcast_to(local_norm.reshape(1, -1), (n_dp, local_norm.size))
    sent = lax.all_to_all(jnp.concatenate([adam_rows, norm_rows], axis=1), "dp", 0, 0, tiled=True)
    dp_sums = jnp.sum(sent, axis=0)

    left_terms, right_terms, pieces = [], [], []
    for (s0, s1), grad_low in zip(bounds, grads):
        b0, b1 = s0 * n_dp, min(s1 * n_dp, count)
        mine = to_owners(grad_low, s1 - s0)
        piece = lax.all_gather(mine, "group", axis=2, tiled=True)
        if s0 == 0:
            dp_sums, piece = lax.optimization_barrier((dp_sums, piece))
        own_rows = lax.dynamic_slice_in_dim(piece, lower, quarter, 1)
        gram_left = jnp.einsum("cim,cjm->cij", piece, own_rows, preferred_element_type=jnp.float32)
        gram_right = jnp.einsum("cim,cij->cmj", piece, mine, preferred_element_type=jnp.float32)
        left_terms.append(to_keepers(gram_left.astype(jnp.bfloat16))[: b1 - b0])
        right_terms.append(to_keepers(gram_right.astype(jnp.bfloat16))[: b1 - b0])
        pieces.append(piece)

    piece = jnp.concatenate(pieces) if len(pieces) > 1 else pieces[0]
    half = jnp.einsum("cim,cmj->cij", piece, right_root, preferred_element_type=jnp.float32)
    half = half.astype(jnp.bfloat16)
    full_left = lax.all_gather(left_root, "group", axis=2, tiled=True)
    direction = jnp.einsum("cim,cmj->cij", full_left, half, preferred_element_type=jnp.float32)
    totals = lax.psum(jnp.concatenate([jnp.sum(direction * direction, axis=(1, 2)), dp_sums[:cap]]), "group")
    direction_sq = totals[:cap]
    adam_owned = totals[cap:]
    ratio = jnp.sqrt(adam_owned / (direction_sq + EPS_GRAFT))
    scaled = (ratio[:, None, None] * direction).astype(jnp.bfloat16)
    scaled, norm_dp = lax.optimization_barrier((scaled, dp_sums[cap:]))
    block_step = to_keepers(scaled)[:count]
    norm_grad = lax.psum(norm_dp, "group").reshape(local_norm.shape)

    new_moment = jnp.concatenate(moments)
    left_term = jnp.concatenate(left_terms).astype(jnp.float32)
    right_term = jnp.concatenate(right_terms).astype(jnp.float32)
    new_left = 0.95 * left_stats + 0.05 * left_term
    new_right = 0.95 * right_stats + 0.05 * right_term
    new_norm_moment = 0.99 * norm_moment + 0.01 * norm_grad * norm_grad
    norm_step = norm_grad / (jnp.sqrt(new_norm_moment) + EPS_ADAM)
    return (block_step, new_moment, new_left, new_right, norm_step, new_norm_moment)


def solution(mesh):
    return jax.shard_map(
        on_device,
        mesh=mesh,
        in_specs=(
            P("group", None, "dp", None),
            P(None, "dp", "group"),
            P(None, "dp", "group"),
            P(None, "dp", "group"),
            P(None, "dp", "group"),
            P(None, "dp", "group"),
            P("dp", "group", None, None),
            P(),
        ),
        out_specs=(
            P(None, "dp", "group"),
            P(None, "dp", "group"),
            P(None, "dp", "group"),
            P(None, "dp", "group"),
            P(),
            P(),
        ),
        check_vma=False,
    )
```

```python
import jax
import jax.numpy as jnp
from jax import lax
from jax.sharding import PartitionSpec as P

EPS_ADAM = 1e-08
EPS_GRAFT = 1e-06


def on_device(
    partials,
    second_moment,
    left_stats,
    right_stats,
    left_roots,
    right_roots,
    norm_partials,
    norm_moment,
):
    n_dp = lax.axis_size("dp")
    me_dp = lax.axis_index("dp")
    me_group = lax.axis_index("group")
    count = second_moment.shape[0]
    rows = partials.shape[2]
    quarter = second_moment.shape[2]
    width = rows * n_dp
    cap = -(-count // n_dp)
    slots = cap * n_dp
    lower = me_group * quarter
    split = (cap + 1) // 2
    bounds = [(0, split), (split, cap)] if cap > 1 else [(0, cap)]

    def to_owners(blocks, n_slots):
        padded = jnp.pad(blocks, ((0, n_slots * n_dp - blocks.shape[0]), (0, 0), (0, 0)))
        sent = lax.all_to_all(padded.reshape(n_slots, n_dp, rows, quarter), "dp", 1, 1, tiled=True)
        return sent.reshape(n_slots, width, quarter)

    def to_keepers(owned):
        n_slots = owned.shape[0]
        back = lax.all_to_all(owned.reshape(n_slots, n_dp, rows, quarter), "dp", 1, 1, tiled=True)
        return back.reshape(n_slots * n_dp, rows, quarter)

    def roots_to_owners(blocks):
        padded = jnp.pad(blocks, ((0, slots - count), (0, 0), (0, 0)))
        return lax.all_to_all(padded.reshape(cap, n_dp, rows, quarter), "dp", 1, 1, tiled=True)

    left_sent = roots_to_owners(left_roots)
    right_sent = roots_to_owners(right_roots)
    local_norm = norm_partials[0, 0]

    grads, moments, adam_parts = [], [], []
    for index, (s0, s1) in enumerate(bounds):
        b0, b1 = s0 * n_dp, min(s1 * n_dp, count)
        grad = lax.psum_scatter(partials[0, b0:b1], "group", scatter_dimension=2, tiled=True)
        low = grad.astype(jnp.bfloat16)
        if index == 0:
            grad, low, left_sent, right_sent = lax.optimization_barrier((grad, low, left_sent, right_sent))
        new_moment = 0.99 * second_moment[b0:b1] + 0.01 * grad * grad
        adam = grad / (jnp.sqrt(new_moment) + EPS_ADAM)
        adam_parts.append(jnp.sum(adam * adam, axis=(1, 2)))
        moments.append(new_moment)
        grads.append(low)

    left_root = left_sent.reshape(cap, width, quarter)
    right_root = right_sent.reshape(cap, width, quarter)

    adam_cat = jnp.pad(jnp.concatenate(adam_parts), (0, slots - count))
    adam_rows = adam_cat.reshape(cap, n_dp).T
    norm_rows = jnp.broadcast_to(local_norm.reshape(1, -1), (n_dp, local_norm.size))
    sent = lax.all_to_all(jnp.concatenate([adam_rows, norm_rows], axis=1), "dp", 0, 0, tiled=True)
    dp_sums = jnp.sum(sent, axis=0)

    left_terms, right_terms, pieces = [], [], []
    for (s0, s1), grad_low in zip(bounds, grads):
        b0, b1 = s0 * n_dp, min(s1 * n_dp, count)
        mine = to_owners(grad_low, s1 - s0)
        piece = lax.all_gather(mine, "group", axis=2, tiled=True)
        if s0 == 0:
            dp_sums, piece = lax.optimization_barrier((dp_sums, piece))
        own_rows = lax.dynamic_slice_in_dim(piece, lower, quarter, 1)
        gram_left = jnp.einsum("cim,cjm->cij", piece, own_rows, preferred_element_type=jnp.float32)
        gram_right = jnp.einsum("cim,cij->cmj", piece, mine, preferred_element_type=jnp.float32)
        left_terms.append(to_keepers(gram_left.astype(jnp.bfloat16))[: b1 - b0])
        right_terms.append(to_keepers(gram_right.astype(jnp.bfloat16))[: b1 - b0])
        pieces.append(piece)

    piece = jnp.concatenate(pieces) if len(pieces) > 1 else pieces[0]
    half = jnp.einsum("cim,cmj->cij", piece, right_root, preferred_element_type=jnp.float32)
    half = half.astype(jnp.bfloat16)
    full_left = lax.all_gather(left_root, "group", axis=2, tiled=True)
    direction = jnp.einsum("cim,cmj->cij", full_left, half, preferred_element_type=jnp.float32)
    totals = lax.psum(jnp.concatenate([jnp.sum(direction * direction, axis=(1, 2)), dp_sums[:cap]]), "group")
    direction_sq = totals[:cap]
    adam_owned = totals[cap:]
    ratio = jnp.sqrt(adam_owned / (direction_sq + EPS_GRAFT))
    scaled = (ratio[:, None, None] * direction).astype(jnp.bfloat16)
    scaled, norm_dp = lax.optimization_barrier((scaled, dp_sums[cap:]))
    block_step = to_keepers(scaled)[:count]
    norm_grad = lax.psum(norm_dp, "group").reshape(local_norm.shape)

    new_moment = jnp.concatenate(moments)
    left_term = jnp.concatenate(left_terms).astype(jnp.float32)
    right_term = jnp.concatenate(right_terms).astype(jnp.float32)
    new_left = 0.95 * left_stats + 0.05 * left_term
    new_right = 0.95 * right_stats + 0.05 * right_term
    new_norm_moment = 0.99 * norm_moment + 0.01 * norm_grad * norm_grad
    norm_step = norm_grad / (jnp.sqrt(new_norm_moment) + EPS_ADAM)
    return (block_step, new_moment, new_left, new_right, norm_step, new_norm_moment)


def solution(mesh):
    return jax.shard_map(
        on_device,
        mesh=mesh,
        in_specs=(
            P("group", None, "dp", None),
            P(None, "dp", "group"),
            P(None, "dp", "group"),
            P(None, "dp", "group"),
            P(None, "dp", "group"),
            P(None, "dp", "group"),
            P("dp", "group", None, None),
            P(),
        ),
        out_specs=(
            P(None, "dp", "group"),
            P(None, "dp", "group"),
            P(None, "dp", "group"),
            P(None, "dp", "group"),
            P(),
            P(),
        ),
        check_vma=False,
    )
```

```python
import jax
import jax.numpy as jnp
from jax import lax
from jax.sharding import PartitionSpec as P

EPS_ADAM = 1e-08
EPS_GRAFT = 1e-06


def on_device(
    partials,
    second_moment,
    left_stats,
    right_stats,
    left_roots,
    right_roots,
    norm_partials,
    norm_moment,
):
    n_dp = lax.axis_size("dp")
    me_dp = lax.axis_index("dp")
    me_group = lax.axis_index("group")
    count = second_moment.shape[0]
    rows = partials.shape[2]
    quarter = second_moment.shape[2]
    width = rows * n_dp
    cap = -(-count // n_dp)
    slots = cap * n_dp
    lower = me_group * quarter
    split = (cap + 1) // 2
    bounds = [(0, split), (split, cap)] if cap > 1 else [(0, cap)]

    def to_owners(blocks, n_slots):
        padded = jnp.pad(blocks, ((0, n_slots * n_dp - blocks.shape[0]), (0, 0), (0, 0)))
        sent = lax.all_to_all(padded.reshape(n_slots, n_dp, rows, quarter), "dp", 1, 1, tiled=True)
        return sent.reshape(n_slots, width, quarter)

    def to_keepers(owned):
        n_slots = owned.shape[0]
        back = lax.all_to_all(owned.reshape(n_slots, n_dp, rows, quarter), "dp", 1, 1, tiled=True)
        return back.reshape(n_slots * n_dp, rows, quarter)

    def roots_to_owners(blocks):
        padded = jnp.pad(blocks, ((0, slots - count), (0, 0), (0, 0)))
        return lax.all_to_all(padded.reshape(cap, n_dp, rows, quarter), "dp", 1, 1, tiled=True)

    left_sent = roots_to_owners(left_roots)
    right_sent = roots_to_owners(right_roots)
    local_norm = norm_partials[0, 0]

    grads, moments, adam_parts = [], [], []
    for index, (s0, s1) in enumerate(bounds):
        b0, b1 = s0 * n_dp, min(s1 * n_dp, count)
        grad = lax.psum_scatter(partials[0, b0:b1], "group", scatter_dimension=2, tiled=True)
        low = grad.astype(jnp.bfloat16)
        if index == 0:
            grad, low, left_sent, right_sent = lax.optimization_barrier((grad, low, left_sent, right_sent))
        new_moment = 0.99 * second_moment[b0:b1] + 0.01 * grad * grad
        adam = grad / (jnp.sqrt(new_moment) + EPS_ADAM)
        adam_parts.append(jnp.sum(adam * adam, axis=(1, 2)))
        moments.append(new_moment)
        grads.append(low)

    left_root = left_sent.reshape(cap, width, quarter)
    right_root = right_sent.reshape(cap, width, quarter)

    adam_cat = jnp.pad(jnp.concatenate(adam_parts), (0, slots - count))
    adam_rows = adam_cat.reshape(cap, n_dp).T
    norm_rows = jnp.broadcast_to(local_norm.reshape(1, -1), (n_dp, local_norm.size))
    sent = lax.all_to_all(jnp.concatenate([adam_rows, norm_rows], axis=1), "dp", 0, 0, tiled=True)
    dp_sums = jnp.sum(sent, axis=0)

    left_terms, right_terms, pieces = [], [], []
    for (s0, s1), grad_low in zip(bounds, grads):
        b0, b1 = s0 * n_dp, min(s1 * n_dp, count)
        mine = to_owners(grad_low, s1 - s0)
        piece = lax.all_gather(mine, "group", axis=2, tiled=True)
        if s0 == 0:
            dp_sums, piece = lax.optimization_barrier((dp_sums, piece))
        own_rows = lax.dynamic_slice_in_dim(piece, lower, quarter, 1)
        gram_left = jnp.einsum("cim,cjm->cij", piece, own_rows, preferred_element_type=jnp.float32)
        gram_right = jnp.einsum("cim,cij->cmj", piece, mine, preferred_element_type=jnp.float32)
        both = jnp.concatenate([gram_left.astype(jnp.bfloat16), gram_right.astype(jnp.bfloat16)])
        back = to_keepers(both)
        n_blocks = (s1 - s0) * n_dp
        left_terms.append(back[: b1 - b0])
        right_terms.append(back[n_blocks : n_blocks + b1 - b0])
        pieces.append(piece)

    piece = jnp.concatenate(pieces) if len(pieces) > 1 else pieces[0]
    half = jnp.einsum("cim,cmj->cij", piece, right_root, preferred_element_type=jnp.float32)
    half = half.astype(jnp.bfloat16)
    full_left = lax.all_gather(left_root, "group", axis=2, tiled=True)
    direction = jnp.einsum("cim,cmj->cij", full_left, half, preferred_element_type=jnp.float32)
    totals = lax.psum(jnp.concatenate([jnp.sum(direction * direction, axis=(1, 2)), dp_sums[:cap]]), "group")
    direction_sq = totals[:cap]
    adam_owned = totals[cap:]
    ratio = jnp.sqrt(adam_owned / (direction_sq + EPS_GRAFT))
    scaled = (ratio[:, None, None] * direction).astype(jnp.bfloat16)
    scaled, norm_dp = lax.optimization_barrier((scaled, dp_sums[cap:]))
    block_step = to_keepers(scaled)[:count]
    norm_grad = lax.psum(norm_dp, "group").reshape(local_norm.shape)

    new_moment = jnp.concatenate(moments)
    left_term = jnp.concatenate(left_terms).astype(jnp.float32)
    right_term = jnp.concatenate(right_terms).astype(jnp.float32)
    new_left = 0.95 * left_stats + 0.05 * left_term
    new_right = 0.95 * right_stats + 0.05 * right_term
    new_norm_moment = 0.99 * norm_moment + 0.01 * norm_grad * norm_grad
    norm_step = norm_grad / (jnp.sqrt(new_norm_moment) + EPS_ADAM)
    return (block_step, new_moment, new_left, new_right, norm_step, new_norm_moment)


def solution(mesh):
    return jax.shard_map(
        on_device,
        mesh=mesh,
        in_specs=(
            P("group", None, "dp", None),
            P(None, "dp", "group"),
            P(None, "dp", "group"),
            P(None, "dp", "group"),
            P(None, "dp", "group"),
            P(None, "dp", "group"),
            P("dp", "group", None, None),
            P(),
        ),
        out_specs=(
            P(None, "dp", "group"),
            P(None, "dp", "group"),
            P(None, "dp", "group"),
            P(None, "dp", "group"),
            P(),
            P(),
        ),
        check_vma=False,
    )
```

```python
import jax
import jax.numpy as jnp
from jax import lax
from jax.sharding import PartitionSpec as P

EPS_ADAM = 1e-08
EPS_GRAFT = 1e-06


def on_device(
    partials,
    second_moment,
    left_stats,
    right_stats,
    left_roots,
    right_roots,
    norm_partials,
    norm_moment,
):
    n_dp = lax.axis_size("dp")
    me_dp = lax.axis_index("dp")
    me_group = lax.axis_index("group")
    count = second_moment.shape[0]
    rows = partials.shape[2]
    quarter = second_moment.shape[2]
    width = rows * n_dp
    cap = -(-count // n_dp)
    slots = cap * n_dp
    lower = me_group * quarter
    split = (cap + 1) // 2
    bounds = [(0, split), (split, cap)] if cap > 1 else [(0, cap)]

    def to_owners(blocks, n_slots):
        padded = jnp.pad(blocks, ((0, n_slots * n_dp - blocks.shape[0]), (0, 0), (0, 0)))
        sent = lax.all_to_all(padded.reshape(n_slots, n_dp, rows, quarter), "dp", 1, 1, tiled=True)
        return sent.reshape(n_slots, width, quarter)

    def to_keepers(owned):
        n_slots = owned.shape[0]
        back = lax.all_to_all(owned.reshape(n_slots, n_dp, rows, quarter), "dp", 1, 1, tiled=True)
        return back.reshape(n_slots * n_dp, rows, quarter)

    def roots_to_owners(blocks):
        padded = jnp.pad(blocks.reshape(2, count, rows, quarter), ((0, 0), (0, slots - count), (0, 0), (0, 0)))
        return lax.all_to_all(padded.reshape(2 * cap, n_dp, rows, quarter), "dp", 1, 1, tiled=True)

    roots_sent = roots_to_owners(jnp.concatenate([left_roots, right_roots]))
    left_sent, right_sent = roots_sent[:cap], roots_sent[cap:]
    local_norm = norm_partials[0, 0]

    grads, moments, adam_parts = [], [], []
    for index, (s0, s1) in enumerate(bounds):
        b0, b1 = s0 * n_dp, min(s1 * n_dp, count)
        grad = lax.psum_scatter(partials[0, b0:b1], "group", scatter_dimension=2, tiled=True)
        low = grad.astype(jnp.bfloat16)
        if index == 0:
            grad, low, left_sent, right_sent = lax.optimization_barrier((grad, low, left_sent, right_sent))
        new_moment = 0.99 * second_moment[b0:b1] + 0.01 * grad * grad
        adam = grad / (jnp.sqrt(new_moment) + EPS_ADAM)
        adam_parts.append(jnp.sum(adam * adam, axis=(1, 2)))
        moments.append(new_moment)
        grads.append(low)

    left_root = left_sent.reshape(cap, width, quarter)
    right_root = right_sent.reshape(cap, width, quarter)

    adam_cat = jnp.pad(jnp.concatenate(adam_parts), (0, slots - count))
    adam_rows = adam_cat.reshape(cap, n_dp).T
    norm_rows = jnp.broadcast_to(local_norm.reshape(1, -1), (n_dp, local_norm.size))
    sent = lax.all_to_all(jnp.concatenate([adam_rows, norm_rows], axis=1), "dp", 0, 0, tiled=True)
    dp_sums = jnp.sum(sent, axis=0)

    left_terms, right_terms, pieces = [], [], []
    for (s0, s1), grad_low in zip(bounds, grads):
        b0, b1 = s0 * n_dp, min(s1 * n_dp, count)
        mine = to_owners(grad_low, s1 - s0)
        piece = lax.all_gather(mine, "group", axis=2, tiled=True)
        if s0 == 0:
            dp_sums, piece = lax.optimization_barrier((dp_sums, piece))
        own_rows = lax.dynamic_slice_in_dim(piece, lower, quarter, 1)
        gram_left = jnp.einsum("cim,cjm->cij", piece, own_rows, preferred_element_type=jnp.float32)
        gram_right = jnp.einsum("cim,cij->cmj", piece, mine, preferred_element_type=jnp.float32)
        both = jnp.concatenate([gram_left.astype(jnp.bfloat16), gram_right.astype(jnp.bfloat16)])
        back = to_keepers(both)
        n_blocks = (s1 - s0) * n_dp
        left_terms.append(back[: b1 - b0])
        right_terms.append(back[n_blocks : n_blocks + b1 - b0])
        pieces.append(piece)

    piece = jnp.concatenate(pieces) if len(pieces) > 1 else pieces[0]
    half = jnp.einsum("cim,cmj->cij", piece, right_root, preferred_element_type=jnp.float32)
    half = half.astype(jnp.bfloat16)
    full_left = lax.all_gather(left_root, "group", axis=2, tiled=True)
    direction = jnp.einsum("cim,cmj->cij", full_left, half, preferred_element_type=jnp.float32)
    totals = lax.psum(jnp.concatenate([jnp.sum(direction * direction, axis=(1, 2)), dp_sums[:cap]]), "group")
    direction_sq = totals[:cap]
    adam_owned = totals[cap:]
    ratio = jnp.sqrt(adam_owned / (direction_sq + EPS_GRAFT))
    scaled = (ratio[:, None, None] * direction).astype(jnp.bfloat16)
    scaled, norm_dp = lax.optimization_barrier((scaled, dp_sums[cap:]))
    block_step = to_keepers(scaled)[:count]
    norm_grad = lax.psum(norm_dp, "group").reshape(local_norm.shape)

    new_moment = jnp.concatenate(moments)
    left_term = jnp.concatenate(left_terms).astype(jnp.float32)
    right_term = jnp.concatenate(right_terms).astype(jnp.float32)
    new_left = 0.95 * left_stats + 0.05 * left_term
    new_right = 0.95 * right_stats + 0.05 * right_term
    new_norm_moment = 0.99 * norm_moment + 0.01 * norm_grad * norm_grad
    norm_step = norm_grad / (jnp.sqrt(new_norm_moment) + EPS_ADAM)
    return (block_step, new_moment, new_left, new_right, norm_step, new_norm_moment)


def solution(mesh):
    return jax.shard_map(
        on_device,
        mesh=mesh,
        in_specs=(
            P("group", None, "dp", None),
            P(None, "dp", "group"),
            P(None, "dp", "group"),
            P(None, "dp", "group"),
            P(None, "dp", "group"),
            P(None, "dp", "group"),
            P("dp", "group", None, None),
            P(),
        ),
        out_specs=(
            P(None, "dp", "group"),
            P(None, "dp", "group"),
            P(None, "dp", "group"),
            P(None, "dp", "group"),
            P(),
            P(),
        ),
        check_vma=False,
    )
```
